128 devices in a mesh: tile: 16 (over z_hi, x, core), lag: 8 (over z_lo, y).
Axes of the slice: x: 4, y: 4, z: 4 (z_hi: 2, z_lo: 2; z = z_hi * 2 + z_lo), core: 2. Of those that a mesh axis runs over, the one named last changes fastest.
Arguments:
- history: bfloat16 [16, 128, 384, 512], P('lag', 'tile'), may hold values from -6 to 6
- lag_blocks: bfloat16 [16, 128, 2, 384, 384], P('lag', 'tile'), may hold values from -0.0625 to 0.0625
- self_inverse: bfloat16 [128, 384, 384], P('tile'), may hold values from -0.3125 to 0.3125
- excitation: float32 [128, 384, 512], P('tile'), may hold values from -6 to 6
- pattern: int32 [16, 128, 2], P('lag', 'tile'), may hold values from 0 to 8
- live_counts: int32 [16, 128], P('lag', 'tile'), may hold values from 1 to 2
Outputs:
- traction: bfloat16 [128, 384, 512], P('tile')
- shifted_history: bfloat16 [16, 128, 384, 512], P('lag', 'tile')
The draws below stay inside these ranges and needn't reach their ends.
All inputs are finite; a program needn't handle non-finite values.
Results may differ from the reference program's by a relative error of at most 0.013.
Values may be sent and summed in bfloat16 or wider, within the bound.
No kernel may reach another device: no remote copies, remote signals or barrier semaphores. Data moves between devices by JAX's collectives and lax.ppermute only.
A program may use at most 128 MiB of HBM per device.

```python
import jax
import jax.numpy as jnp
from jax import lax

VEC = 384
LAG_DEV = 2
EXCITE = 512
SLOTS = 2
EDGE = 4
BLOCKS = 128
LAGS = 16
N_LAG = 8


def draw_pattern(key, part):
    width = 2 * EDGE + 1
    first_key, second_key = jax.random.split(jax.random.fold_in(key, 11))
    base = jax.random.randint(first_key, (LAGS, BLOCKS, 1), 0, width, dtype=jnp.int32)
    stride = jax.random.randint(second_key, (LAGS, BLOCKS, 1), 1, width, dtype=jnp.int32)
    row_ids = jnp.arange(LAGS, dtype=jnp.int32)[:, None, None] * BLOCKS + jnp.arange(BLOCKS, dtype=jnp.int32)[None, :, None]
    base = jnp.where(row_ids == 0, width - 1, base)
    base = jnp.where(row_ids == 1, 0, base)
    slot_ids = jnp.arange(SLOTS, dtype=jnp.int32)[None, None, :]
    return ((base + slot_ids * stride) % width).astype(jnp.int32)


def place_ends(values, stream_key, least, largest):
    index_at = [jax.random.randint(jax.random.fold_in(stream_key, axis), (), 0, length) for axis, length in enumerate(values.shape)]
    main_axis = values.shape.index(max(values.shape))
    next_to = index_at[:main_axis] + [(index_at[main_axis] + 1) % values.shape[main_axis]] + index_at[main_axis + 1:]
    return values.at[tuple(index_at)].set(least).at[tuple(next_to)].set(largest)


def block_levels(stream_key, dims, cuts, least, high):
    level = 1.0
    for position, parts in cuts:
        draws = jax.random.uniform(jax.random.fold_in(jax.random.fold_in(stream_key, 6), position), (parts,), jnp.float32, least / len(cuts), high / len(cuts))
        level = level * jnp.repeat(jnp.exp(draws), dims[position] // parts).reshape((-1,) + (1,) * (len(dims) - 1 - position))
    return level


def bell_draw(rng, dims, scale, bound, shards=(), kind=jnp.bfloat16):
    result = scale * jax.random.normal(rng, dims, jnp.float32)
    if shards:
        result = result * block_levels(rng, dims, shards, -0.22, 0.18)
    return jnp.clip(result, -bound, bound).astype(kind)


def setup_inputs(seed: int = 0) -> dict:
    arg_keys = jax.random.split(jax.random.key(seed), 7)
    return {
        "history": bell_draw(arg_keys[0], (LAGS, BLOCKS, VEC, EXCITE), 1.0, 6.0, ((0, 8), (1, 16))),
        "lag_blocks": bell_draw(arg_keys[1], (LAGS, BLOCKS, SLOTS, VEC, VEC), (VEC * LAGS * 3 // 2) ** -0.5, 0.0625, ((0, 8), (1, 16))),
        "self_inverse": bell_draw(arg_keys[2], (BLOCKS, VEC, VEC), VEC ** -0.5, 0.3125, ((0, 16),)),
        "excitation": bell_draw(arg_keys[3], (BLOCKS, VEC, EXCITE), 1.0, 6.0, ((0, 16),), jnp.float32),
        "pattern": draw_pattern(jax.random.fold_in(arg_keys[6], 71), 0),
        "live_counts": place_ends(jax.random.randint(arg_keys[5], (LAGS, BLOCKS), 1, SLOTS + 1), jax.random.fold_in(arg_keys[5], 1), 1, SLOTS).astype(jnp.int32),
    }


def lag_term(history, lag_blocks, pattern, live_counts, lag):
    positions = jnp.arange(BLOCKS, dtype=jnp.int32)
    source_index = (positions[:, None] + pattern[lag] - EDGE) % BLOCKS
    live = jnp.arange(SLOTS, dtype=jnp.int32)[None, :] < live_counts[lag][:, None]
    sources = history[lag][source_index] * live[:, :, None, None].astype(history.dtype)
    return jnp.einsum("bsij,bsjr->bir", lag_blocks[lag].astype(jnp.float32), sources.astype(jnp.float32))


def reference(history, lag_blocks, self_inverse, excitation, pattern, live_counts):
    def group_term(group):
        def one_lag(offset):
            return lag_term(history, lag_blocks, pattern, live_counts, group * LAG_DEV + offset)
        terms = lax.map(one_lag, jnp.arange(LAG_DEV, dtype=jnp.int32))
        return jnp.sum(terms, axis=0).astype(jnp.bfloat16)

    partials = lax.map(group_term, jnp.arange(N_LAG, dtype=jnp.int32))
    field = jnp.sum(partials.astype(jnp.float32), axis=0)
    residual = (excitation - field).astype(jnp.bfloat16)
    traction = jnp.einsum("bij,bjr->bir", self_inverse.astype(jnp.float32), residual.astype(jnp.float32)).astype(jnp.bfloat16)
    shifted_history = jnp.concatenate([traction[None], history[:-1]], axis=0)
    return (traction, shifted_history)
```

```python
import jax
import jax.numpy as jnp
from jax import lax
from jax.experimental import pallas as pl
from jax.experimental.pallas import tpu as pltpu
from jax.sharding import PartitionSpec as P

EDGE = 4


def term_kernel(src_ref, cnt_ref, a_ref, l0, m0, r0, l1, m1, r1, out_ref, acc_ref):
    b = pl.program_id(0)
    l = pl.program_id(1)
    blocks = pl.num_programs(0)

    @pl.when(l == 0)
    def _():
        acc_ref[...] = jnp.zeros_like(acc_ref)

    cnt = cnt_ref[l, b]
    for s, (lf, md, rt) in enumerate(((l0, m0, r0), (l1, m1, r1))):
        w = src_ref[l, b, s]
        live = s < cnt
        for ref, cond in ((lf, w < EDGE), (md, (w >= EDGE) & (w < EDGE + blocks)), (rt, w >= EDGE + blocks)):
            @pl.when(live & cond)
            def _():
                acc_ref[...] += jnp.dot(a_ref[s], ref[...], preferred_element_type=jnp.float32)

    @pl.when(l == pl.num_programs(1) - 1)
    def _():
        out_ref[...] = acc_ref[...].astype(out_ref.dtype)


def lag_partial(history, left, right, lag_blocks, pattern, live_counts):
    lags, blocks, vec, ex = history.shape
    slots = lag_blocks.shape[2]
    window = jnp.arange(blocks, dtype=jnp.int32)[None, :, None] + pattern

    def local_spec(s):
        return pl.BlockSpec((None, None, vec, ex), lambda b, l, src, cnt: (l, jnp.clip(src[l, b, s] - EDGE, 0, blocks - 1), 0, 0))

    def left_spec(s):
        return pl.BlockSpec((None, None, vec, ex), lambda b, l, src, cnt: (l, jnp.clip(src[l, b, s], 0, EDGE - 1), 0, 0))

    def right_spec(s):
        return pl.BlockSpec((None, None, vec, ex), lambda b, l, src, cnt: (l, jnp.clip(src[l, b, s] - EDGE - blocks, 0, EDGE - 1), 0, 0))

    in_specs = [pl.BlockSpec((None, None, slots, vec, vec), lambda b, l, src, cnt: (l, b, 0, 0, 0))]
    operands = [lag_blocks]
    for s in range(slots):
        in_specs += [left_spec(s), local_spec(s), right_spec(s)]
        operands += [left, history, right]
    grid_spec = pltpu.PrefetchScalarGridSpec(
        num_scalar_prefetch=2,
        grid=(blocks, lags),
        in_specs=in_specs,
        out_specs=pl.BlockSpec((None, vec, ex), lambda b, l, src, cnt: (b, 0, 0)),
        scratch_shapes=[pltpu.VMEM((vec, ex), jnp.float32)],
    )
    flops = 2 * lags * blocks * slots * vec * vec * ex
    moved = 2 * (lag_blocks.size + slots * history.size + blocks * vec * ex)
    return pl.pallas_call(
        term_kernel,
        grid_spec=grid_spec,
        out_shape=jax.ShapeDtypeStruct((blocks, vec, ex), jnp.bfloat16),
        cost_estimate=pl.CostEstimate(flops=flops, transcendentals=0, bytes_accessed=moved),
    )(window, live_counts, *operands)


def shifted_by(array, axis, by):
    count = lax.axis_size(axis)
    return lax.ppermute(array, axis, [(i, (i + by) % count) for i in range(count)])


def passed_along(array, axis, by):
    length = lax.axis_size(axis)
    pairs = [(i, i + by) for i in range(length) if 0 <= i + by < length]
    return lax.ppermute(array, axis, pairs)


def shards(history, lag_blocks, self_inverse, excitation, pattern, live_counts):
    blocks_here = history.shape[1]
    carried = passed_along(history[-1], "lag", 1)
    left = shifted_by(history[:, blocks_here - EDGE:], "tile", 1)
    right = shifted_by(history[:, :EDGE], "tile", -1)
    live = jnp.minimum(live_counts, lag_blocks.shape[2])
    partial = lag_partial(history, left, right, lag_blocks, pattern, live)

    n_lag = lax.axis_size("lag")
    me = lax.axis_index("lag")
    field = lax.dynamic_index_in_dim(partial, me, 0, keepdims=False).astype(jnp.float32)
    for k in range(1, n_lag):
        piece = lax.dynamic_index_in_dim(partial, (me + k) % n_lag, 0, keepdims=False)
        field = field + shifted_by(piece, "lag", k).astype(jnp.float32)
    mine = lax.dynamic_index_in_dim(excitation, me, 0, keepdims=False)
    residual = (mine - field).astype(jnp.bfloat16)
    inverse = lax.dynamic_index_in_dim(self_inverse, me, 0, keepdims=False)
    block = jnp.dot(inverse, residual, preferred_element_type=jnp.float32).astype(jnp.bfloat16)

    gathered = [block] + [shifted_by(block, "lag", k) for k in range(1, n_lag)]
    ordered = jnp.stack(gathered[::-1])
    traction = jnp.roll(ordered, me + 1, axis=0)

    newest = jnp.where(me == 0, traction, carried)
    shifted_history = jnp.concatenate([newest[None], history[:-1]], axis=0)
    return (traction, shifted_history)


def solution(mesh):
    in_specs = (
        P("lag", "tile", None, None),
        P("lag", "tile", None, None, None),
        P("tile", None, None),
        P("tile", None, None),
        P("lag", "tile", None),
        P("lag", "tile"),
    )
    out_specs = (P("tile", None, None), P("lag", "tile", None, None))
    return jax.shard_map(shards, mesh=mesh, in_specs=in_specs, out_specs=out_specs, check_vma=False)
```

```python
import jax
import jax.numpy as jnp
from jax import lax
from jax.experimental import pallas as pl
from jax.experimental.pallas import tpu as pltpu
from jax.sharding import PartitionSpec as P

EDGE = 4


def term_kernel(src_ref, cnt_ref, a_ref, l0, m0, r0, l1, m1, r1, out_ref, acc_ref):
    b = pl.program_id(0)
    l = pl.program_id(1)
    blocks = pl.num_programs(0)

    @pl.when(l == 0)
    def _():
        acc_ref[...] = jnp.zeros_like(acc_ref)

    cnt = cnt_ref[l, b]
    for s, (lf, md, rt) in enumerate(((l0, m0, r0), (l1, m1, r1))):
        w = src_ref[l, b, s]
        live = s < cnt
        for ref, cond in ((lf, w < EDGE), (md, (w >= EDGE) & (w < EDGE + blocks)), (rt, w >= EDGE + blocks)):
            @pl.when(live & cond)
            def _():
                acc_ref[...] += jnp.dot(a_ref[s], ref[...], preferred_element_type=jnp.float32)

    @pl.when(l == pl.num_programs(1) - 1)
    def _():
        out_ref[...] = acc_ref[...].astype(out_ref.dtype)


def lag_partial(history, left, right, lag_blocks, pattern, live_counts):
    lags, blocks, vec, ex = history.shape
    slots = lag_blocks.shape[2]
    window = jnp.arange(blocks, dtype=jnp.int32)[None, :, None] + pattern

    def used(src, cnt, l, b, s, lo, hi):
        w = src[l, b, s]
        return (s < cnt[l, b]) & (w >= lo) & (w < hi), w - lo

    def source_spec(s, lo, hi, count):
        def index(b, l, src, cnt):
            on, at = used(src, cnt, l, b, s, lo, hi)
            return (jnp.where(on, l, 0), jnp.where(on, jnp.clip(at, 0, count - 1), 0), 0, 0)
        return pl.BlockSpec((None, None, vec, ex), index)

    def local_spec(s):
        return source_spec(s, EDGE, EDGE + blocks, blocks)

    def left_spec(s):
        return source_spec(s, 0, EDGE, EDGE)

    def right_spec(s):
        return source_spec(s, EDGE + blocks, 2 * EDGE + blocks, EDGE)

    in_specs = [pl.BlockSpec((None, None, slots, vec, vec), lambda b, l, src, cnt: (l, b, 0, 0, 0))]
    operands = [lag_blocks]
    for s in range(slots):
        in_specs += [left_spec(s), local_spec(s), right_spec(s)]
        operands += [left, history, right]
    grid_spec = pltpu.PrefetchScalarGridSpec(
        num_scalar_prefetch=2,
        grid=(blocks, lags),
        in_specs=in_specs,
        out_specs=pl.BlockSpec((None, vec, ex), lambda b, l, src, cnt: (b, 0, 0)),
        scratch_shapes=[pltpu.VMEM((vec, ex), jnp.float32)],
    )
    flops = 2 * lags * blocks * slots * vec * vec * ex
    moved = 2 * (lag_blocks.size + slots * history.size + blocks * vec * ex)
    return pl.pallas_call(
        term_kernel,
        grid_spec=grid_spec,
        out_shape=jax.ShapeDtypeStruct((blocks, vec, ex), jnp.bfloat16),
        cost_estimate=pl.CostEstimate(flops=flops, transcendentals=0, bytes_accessed=moved),
    )(window, live_counts, *operands)


def shifted_by(array, axis, by):
    count = lax.axis_size(axis)
    return lax.ppermute(array, axis, [(i, (i + by) % count) for i in range(count)])


def passed_along(array, axis, by):
    length = lax.axis_size(axis)
    pairs = [(i, i + by) for i in range(length) if 0 <= i + by < length]
    return lax.ppermute(array, axis, pairs)


def shards(history, lag_blocks, self_inverse, excitation, pattern, live_counts):
    blocks_here = history.shape[1]
    carried = passed_along(history[-1], "lag", 1)
    left = shifted_by(history[:, blocks_here - EDGE:], "tile", 1)
    right = shifted_by(history[:, :EDGE], "tile", -1)
    live = jnp.minimum(live_counts, lag_blocks.shape[2])
    partial = lag_partial(history, left, right, lag_blocks, pattern, live)
    partial, carried = lax.optimization_barrier((partial, carried))

    n_lag = lax.axis_size("lag")
    me = lax.axis_index("lag")
    field = lax.dynamic_index_in_dim(partial, me, 0, keepdims=False).astype(jnp.float32)
    for k in range(1, n_lag):
        piece = lax.dynamic_index_in_dim(partial, (me + k) % n_lag, 0, keepdims=False)
        field = field + shifted_by(piece, "lag", k).astype(jnp.float32)
    mine = lax.dynamic_index_in_dim(excitation, me, 0, keepdims=False)
    residual = (mine - field).astype(jnp.bfloat16)
    inverse = lax.dynamic_index_in_dim(self_inverse, me, 0, keepdims=False)
    block = jnp.dot(inverse, residual, preferred_element_type=jnp.float32).astype(jnp.bfloat16)

    gathered = [block] + [shifted_by(block, "lag", k) for k in range(1, n_lag)]
    ordered = jnp.stack(gathered[::-1])
    traction = jnp.roll(ordered, me + 1, axis=0)

    newest = jnp.where(me == 0, traction, carried)
    shifted_history = jnp.concatenate([newest[None], history[:-1]], axis=0)
    return (traction, shifted_history)


def solution(mesh):
    in_specs = (
        P("lag", "tile", None, None),
        P("lag", "tile", None, None, None),
        P("tile", None, None),
        P("tile", None, None),
        P("lag", "tile", None),
        P("lag", "tile"),
    )
    out_specs = (P("tile", None, None), P("lag", "tile", None, None))
    return jax.shard_map(shards, mesh=mesh, in_specs=in_specs, out_specs=out_specs, check_vma=False)
```

```python
import jax
import jax.numpy as jnp
from jax import lax
from jax.experimental import pallas as pl
from jax.experimental.pallas import tpu as pltpu
from jax.sharding import PartitionSpec as P

EDGE = 4


def term_kernel(src_ref, cnt_ref, a_ref, l0, m0, r0, l1, m1, r1, out_ref, acc_ref):
    b = pl.program_id(0)
    l = pl.program_id(1)
    blocks = pl.num_programs(0)

    @pl.when(l == 0)
    def _():
        acc_ref[...] = jnp.zeros_like(acc_ref)

    cnt = cnt_ref[l, b]
    for s, (lf, md, rt) in enumerate(((l0, m0, r0), (l1, m1, r1))):
        w = src_ref[l, b, s]
        live = s < cnt
        for ref, cond in ((lf, w < EDGE), (md, (w >= EDGE) & (w < EDGE + blocks)), (rt, w >= EDGE + blocks)):
            @pl.when(live & cond)
            def _():
                acc_ref[...] += jnp.dot(a_ref[s], ref[...], preferred_element_type=jnp.float32)

    @pl.when(l == pl.num_programs(1) - 1)
    def _():
        out_ref[...] = acc_ref[...].astype(out_ref.dtype)


def lag_partial(history, left, right, lag_blocks, pattern, live_counts, column):
    lags, blocks, vec, _ = history.shape
    ex = left.shape[-1]
    slots = lag_blocks.shape[2]
    window = jnp.arange(blocks, dtype=jnp.int32)[None, :, None] + pattern

    def used(src, cnt, l, b, s, lo, hi):
        w = src[l, b, s]
        return (s < cnt[l, b]) & (w >= lo) & (w < hi), w - lo

    def source_spec(s, lo, hi, count, col):
        def index(b, l, src, cnt):
            on, at = used(src, cnt, l, b, s, lo, hi)
            return (jnp.where(on, l, 0), jnp.where(on, jnp.clip(at, 0, count - 1), 0), 0, col)
        return pl.BlockSpec((None, None, vec, ex), index)

    def local_spec(s):
        return source_spec(s, EDGE, EDGE + blocks, blocks, column)

    def left_spec(s):
        return source_spec(s, 0, EDGE, EDGE, 0)

    def right_spec(s):
        return source_spec(s, EDGE + blocks, 2 * EDGE + blocks, EDGE, 0)

    in_specs = [pl.BlockSpec((None, None, slots, vec, vec), lambda b, l, src, cnt: (l, b, 0, 0, 0))]
    operands = [lag_blocks]
    for s in range(slots):
        in_specs += [left_spec(s), local_spec(s), right_spec(s)]
        operands += [left, history, right]
    grid_spec = pltpu.PrefetchScalarGridSpec(
        num_scalar_prefetch=2,
        grid=(blocks, lags),
        in_specs=in_specs,
        out_specs=pl.BlockSpec((None, vec, ex), lambda b, l, src, cnt: (b, 0, 0)),
        scratch_shapes=[pltpu.VMEM((vec, ex), jnp.float32)],
    )
    flops = 2 * lags * blocks * slots * vec * vec * ex
    moved = 2 * (lag_blocks.size + slots * lags * blocks * vec * ex + blocks * vec * ex)
    return pl.pallas_call(
        term_kernel,
        grid_spec=grid_spec,
        out_shape=jax.ShapeDtypeStruct((blocks, vec, ex), jnp.bfloat16),
        cost_estimate=pl.CostEstimate(flops=flops, transcendentals=0, bytes_accessed=moved),
    )(window, live_counts, *operands)


def shifted_by(array, axis, by):
    count = lax.axis_size(axis)
    return lax.ppermute(array, axis, [(i, (i + by) % count) for i in range(count)])


def passed_along(array, axis, by):
    length = lax.axis_size(axis)
    pairs = [(i, i + by) for i in range(length) if 0 <= i + by < length]
    return lax.ppermute(array, axis, pairs)


def lag_sum(partial, excitation, self_inverse):
    n_lag = lax.axis_size("lag")
    me = lax.axis_index("lag")
    field = lax.dynamic_index_in_dim(partial, me, 0, keepdims=False).astype(jnp.float32)
    for k in range(1, n_lag):
        piece = lax.dynamic_index_in_dim(partial, (me + k) % n_lag, 0, keepdims=False)
        field = field + shifted_by(piece, "lag", k).astype(jnp.float32)
    mine = lax.dynamic_index_in_dim(excitation, me, 0, keepdims=False)
    residual = (mine - field).astype(jnp.bfloat16)
    inverse = lax.dynamic_index_in_dim(self_inverse, me, 0, keepdims=False)
    block = jnp.dot(inverse, residual, preferred_element_type=jnp.float32).astype(jnp.bfloat16)
    gathered = [block] + [shifted_by(block, "lag", k) for k in range(1, n_lag)]
    ordered = jnp.stack(gathered[::-1])
    return jnp.roll(ordered, me + 1, axis=0)


CHUNKS = 2


def shards(history, lag_blocks, self_inverse, excitation, pattern, live_counts):
    blocks_here = history.shape[1]
    width = history.shape[-1] // CHUNKS
    carried = passed_along(history[-1], "lag", 1)
    live = jnp.minimum(live_counts, lag_blocks.shape[2])
    me = lax.axis_index("lag")
    pieces = []
    for c in range(CHUNKS):
        cols = slice(c * width, (c + 1) * width)
        tail = history[:, blocks_here - EDGE:, :, cols]
        head = history[:, :EDGE, :, cols]
        if c:
            tail, head, _, _ = lax.optimization_barrier((tail, head, left, right))
        left = shifted_by(tail, "tile", 1)
        right = shifted_by(head, "tile", -1)
        partial = lag_partial(history, left, right, lag_blocks, pattern, live, c)
        if c == CHUNKS - 1:
            partial, carried = lax.optimization_barrier((partial, carried))
        pieces.append(lag_sum(partial, excitation[..., cols], self_inverse))
    traction = jnp.concatenate(pieces, axis=-1)

    newest = jnp.where(me == 0, traction, carried)
    shifted_history = jnp.concatenate([newest[None], history[:-1]], axis=0)
    return (traction, shifted_history)


def solution(mesh):
    in_specs = (
        P("lag", "tile", None, None),
        P("lag", "tile", None, None, None),
        P("tile", None, None),
        P("tile", None, None),
        P("lag", "tile", None),
        P("lag", "tile"),
    )
    out_specs = (P("tile", None, None), P("lag", "tile", None, None))
    return jax.shard_map(shards, mesh=mesh, in_specs=in_specs, out_specs=out_specs, check_vma=False)
```

```python
import jax
import jax.numpy as jnp
from jax import lax
from jax.experimental import pallas as pl
from jax.experimental.pallas import tpu as pltpu
from jax.sharding import PartitionSpec as P

EDGE = 4


def term_kernel(src_ref, cnt_ref, a_ref, l0, m0, r0, l1, m1, r1, out_ref, acc_ref):
    b = pl.program_id(0)
    l = pl.program_id(1)
    blocks = pl.num_programs(0)

    @pl.when(l == 0)
    def _():
        acc_ref[...] = jnp.zeros_like(acc_ref)

    cnt = cnt_ref[l, b]
    for s, (lf, md, rt) in enumerate(((l0, m0, r0), (l1, m1, r1))):
        w = src_ref[l, b, s]
        live = s < cnt
        for ref, cond in ((lf, w < EDGE), (md, (w >= EDGE) & (w < EDGE + blocks)), (rt, w >= EDGE + blocks)):
            @pl.when(live & cond)
            def _():
                acc_ref[...] += jnp.dot(a_ref[s], ref[...], preferred_element_type=jnp.float32)

    @pl.when(l == pl.num_programs(1) - 1)
    def _():
        out_ref[...] = acc_ref[...].astype(out_ref.dtype)


def lag_partial(history, left, right, lag_blocks, pattern, live_counts):
    lags, blocks, vec, ex = history.shape
    slots = lag_blocks.shape[2]
    window = jnp.arange(blocks, dtype=jnp.int32)[None, :, None] + pattern

    def used(src, cnt, l, b, s, lo, hi):
        w = src[l, b, s]
        return (s < cnt[l, b]) & (w >= lo) & (w < hi), w - lo

    def source_spec(s, lo, hi, count):
        def index(b, l, src, cnt):
            on, at = used(src, cnt, l, b, s, lo, hi)
            return (jnp.where(on, l, 0), jnp.where(on, jnp.clip(at, 0, count - 1), 0), 0, 0)
        return pl.BlockSpec((None, None, vec, ex), index)

    def local_spec(s):
        return source_spec(s, EDGE, EDGE + blocks, blocks)

    def left_spec(s):
        return source_spec(s, 0, EDGE, EDGE)

    def right_spec(s):
        return source_spec(s, EDGE + blocks, 2 * EDGE + blocks, EDGE)

    in_specs = [pl.BlockSpec((None, None, slots, vec, vec), lambda b, l, src, cnt: (l, b, 0, 0, 0))]
    operands = [lag_blocks]
    for s in range(slots):
        in_specs += [left_spec(s), local_spec(s), right_spec(s)]
        operands += [left, history, right]
    grid_spec = pltpu.PrefetchScalarGridSpec(
        num_scalar_prefetch=2,
        grid=(blocks, lags),
        in_specs=in_specs,
        out_specs=pl.BlockSpec((None, vec, ex), lambda b, l, src, cnt: (b, 0, 0)),
        scratch_shapes=[pltpu.VMEM((vec, ex), jnp.float32)],
    )
    flops = 2 * lags * blocks * slots * vec * vec * ex
    moved = 2 * (lag_blocks.size + slots * history.size + blocks * vec * ex)
    return pl.pallas_call(
        term_kernel,
        grid_spec=grid_spec,
        out_shape=jax.ShapeDtypeStruct((blocks, vec, ex), jnp.bfloat16),
        cost_estimate=pl.CostEstimate(flops=flops, transcendentals=0, bytes_accessed=moved),
    )(window, live_counts, *operands)


def shifted_by(array, axis, by):
    count = lax.axis_size(axis)
    return lax.ppermute(array, axis, [(i, (i + by) % count) for i in range(count)])


def passed_along(array, axis, by):
    length = lax.axis_size(axis)
    pairs = [(i, i + by) for i in range(length) if 0 <= i + by < length]
    return lax.ppermute(array, axis, pairs)


def shards(history, lag_blocks, self_inverse, excitation, pattern, live_counts):
    blocks_here = history.shape[1]
    carried = passed_along(history[-1], "lag", 1)
    left = shifted_by(history[:, blocks_here - EDGE:], "tile", 1)
    right = shifted_by(history[:, :EDGE], "tile", -1)
    live = jnp.minimum(live_counts, lag_blocks.shape[2])
    partial = lag_partial(history, left, right, lag_blocks, pattern, live)
    partial, carried = lax.optimization_barrier((partial, carried))

    n_lag = lax.axis_size("lag")
    ny = n_lag // 2
    me = lax.axis_index("lag")
    zl, y = me // ny, me % ny
    rows = partial.reshape((2, ny) + partial.shape[1:])

    def along_y(d):
        return [(i, (i // ny) * ny + (i % ny + d) % ny) for i in range(n_lag)]

    across_z = [(i, (1 - i // ny) * ny + i % ny) for i in range(n_lag)]
    column = lax.dynamic_index_in_dim(rows, y, 1, keepdims=False).astype(jnp.float32)
    for d in range(1, ny):
        piece = lax.dynamic_index_in_dim(rows, (y + d) % ny, 1, keepdims=False)
        column = column + lax.ppermute(piece, "lag", along_y(d)).astype(jnp.float32)
    theirs = lax.dynamic_index_in_dim(column, 1 - zl, 0, keepdims=False).astype(jnp.bfloat16)
    field = lax.dynamic_index_in_dim(column, zl, 0, keepdims=False)
    field = field + lax.ppermute(theirs, "lag", across_z).astype(jnp.float32)

    mine = lax.dynamic_index_in_dim(excitation, me, 0, keepdims=False)
    residual = (mine - field).astype(jnp.bfloat16)
    inverse = lax.dynamic_index_in_dim(self_inverse, me, 0, keepdims=False)
    block = jnp.dot(inverse, residual, preferred_element_type=jnp.float32).astype(jnp.bfloat16)

    partner = lax.ppermute(block, "lag", across_z)
    pair = jnp.where(zl == 0, jnp.stack([block, partner]), jnp.stack([partner, block]))
    columns = [pair] + [lax.ppermute(pair, "lag", along_y(d)) for d in range(1, ny)]
    ordered = jnp.stack(columns[::-1], axis=1)
    traction = jnp.roll(ordered, y + 1, axis=1).reshape(partial.shape)

    newest = jnp.where(me == 0, traction, carried)
    shifted_history = jnp.concatenate([newest[None], history[:-1]], axis=0)
    return (traction, shifted_history)


def solution(mesh):
    in_specs = (
        P("lag", "tile", None, None),
        P("lag", "tile", None, None, None),
        P("tile", None, None),
        P("tile", None, None),
        P("lag", "tile", None),
        P("lag", "tile"),
    )
    out_specs = (P("tile", None, None), P("lag", "tile", None, None))
    return jax.shard_map(shards, mesh=mesh, in_specs=in_specs, out_specs=out_specs, check_vma=False)
```

```python
import jax
import jax.numpy as jnp
from jax import lax
from jax.experimental import pallas as pl
from jax.experimental.pallas import tpu as pltpu
from jax.sharding import PartitionSpec as P

EDGE = 4


def term_kernel(src_ref, cnt_ref, a_ref, l0, m0, r0, l1, m1, r1, out_ref, acc_ref):
    b = pl.program_id(0)
    l = pl.program_id(1)
    blocks = pl.num_programs(0)

    @pl.when(l == 0)
    def _():
        acc_ref[...] = jnp.zeros_like(acc_ref)

    cnt = cnt_ref[l, b]
    for s, (lf, md, rt) in enumerate(((l0, m0, r0), (l1, m1, r1))):
        w = src_ref[l, b, s]
        live = s < cnt
        for ref, cond in ((lf, w < EDGE), (md, (w >= EDGE) & (w < EDGE + blocks)), (rt, w >= EDGE + blocks)):
            @pl.when(live & cond)
            def _():
                acc_ref[...] += jnp.dot(a_ref[s], ref[...], preferred_element_type=jnp.float32)

    @pl.when(l == pl.num_programs(1) - 1)
    def _():
        out_ref[...] = acc_ref[...].astype(out_ref.dtype)


def lag_partial(history, left, right, lag_blocks, pattern, live_counts):
    lags, blocks, vec, ex = history.shape
    slots = lag_blocks.shape[2]
    window = jnp.arange(blocks, dtype=jnp.int32)[None, :, None] + pattern

    def used(src, cnt, l, b, s, lo, hi):
        w = src[l, b, s]
        return (s < cnt[l, b]) & (w >= lo) & (w < hi), w - lo

    def source_spec(s, lo, hi, count):
        def index(b, l, src, cnt):
            on, at = used(src, cnt, l, b, s, lo, hi)
            return (jnp.where(on, l, 0), jnp.where(on, jnp.clip(at, 0, count - 1), 0), 0, 0)
        return pl.BlockSpec((None, None, vec, ex), index)

    def local_spec(s):
        return source_spec(s, EDGE, EDGE + blocks, blocks)

    def left_spec(s):
        return source_spec(s, 0, EDGE, EDGE)

    def right_spec(s):
        return source_spec(s, EDGE + blocks, 2 * EDGE + blocks, EDGE)

    in_specs = [pl.BlockSpec((None, None, slots, vec, vec), lambda b, l, src, cnt: (l, b, 0, 0, 0))]
    operands = [lag_blocks]
    for s in range(slots):
        in_specs += [left_spec(s), local_spec(s), right_spec(s)]
        operands += [left, history, right]
    grid_spec = pltpu.PrefetchScalarGridSpec(
        num_scalar_prefetch=2,
        grid=(blocks, lags),
        in_specs=in_specs,
        out_specs=pl.BlockSpec((None, vec, ex), lambda b, l, src, cnt: (b, 0, 0)),
        scratch_shapes=[pltpu.VMEM((vec, ex), jnp.float32)],
    )
    flops = 2 * lags * blocks * slots * vec * vec * ex
    moved = 2 * (lag_blocks.size + slots * history.size + blocks * vec * ex)
    return pl.pallas_call(
        term_kernel,
        grid_spec=grid_spec,
        out_shape=jax.ShapeDtypeStruct((blocks, vec, ex), jnp.bfloat16),
        cost_estimate=pl.CostEstimate(flops=flops, transcendentals=0, bytes_accessed=moved),
    )(window, live_counts, *operands)


def shifted_by(array, axis, by):
    count = lax.axis_size(axis)
    return lax.ppermute(array, axis, [(i, (i + by) % count) for i in range(count)])


def passed_along(array, axis, by):
    length = lax.axis_size(axis)
    pairs = [(i, i + by) for i in range(length) if 0 <= i + by < length]
    return lax.ppermute(array, axis, pairs)


def shards(history, lag_blocks, self_inverse, excitation, pattern, live_counts):
    blocks_here = history.shape[1]
    left = shifted_by(history[:, blocks_here - EDGE:], "tile", 1)
    right = shifted_by(history[:, :EDGE], "tile", -1)
    oldest, left, right = lax.optimization_barrier((history[-1], left, right))
    carried = passed_along(oldest, "lag", 1)
    live = jnp.minimum(live_counts, lag_blocks.shape[2])
    partial = lag_partial(history, left, right, lag_blocks, pattern, live)

    n_lag = lax.axis_size("lag")
    me = lax.axis_index("lag")
    field = lax.dynamic_index_in_dim(partial, me, 0, keepdims=False).astype(jnp.float32)
    for k in range(1, n_lag):
        piece = lax.dynamic_index_in_dim(partial, (me + k) % n_lag, 0, keepdims=False)
        field = field + shifted_by(piece, "lag", k).astype(jnp.float32)
    mine = lax.dynamic_index_in_dim(excitation, me, 0, keepdims=False)
    residual = (mine - field).astype(jnp.bfloat16)
    inverse = lax.dynamic_index_in_dim(self_inverse, me, 0, keepdims=False)
    block = jnp.dot(inverse, residual, preferred_element_type=jnp.float32).astype(jnp.bfloat16)
    block, carried = lax.optimization_barrier((block, carried))

    gathered = [block] + [shifted_by(block, "lag", k) for k in range(1, n_lag)]
    ordered = jnp.stack(gathered[::-1])
    traction = jnp.roll(ordered, me + 1, axis=0)

    newest = jnp.where(me == 0, traction, carried)
    shifted_history = jnp.concatenate([newest[None], history[:-1]], axis=0)
    return (traction, shifted_history)


def solution(mesh):
    in_specs = (
        P("lag", "tile", None, None),
        P("lag", "tile", None, None, None),
        P("tile", None, None),
        P("tile", None, None),
        P("lag", "tile", None),
        P("lag", "tile"),
    )
    out_specs = (P("tile", None, None), P("lag", "tile", None, None))
    return jax.shard_map(shards, mesh=mesh, in_specs=in_specs, out_specs=out_specs, check_vma=False)
```

```python
import jax
import jax.numpy as jnp
from jax import lax
from jax.experimental import pallas as pl
from jax.experimental.pallas import tpu as pltpu
from jax.sharding import PartitionSpec as P

EDGE = 4


def term_kernel(src_ref, cnt_ref, a_ref, l0, m0, r0, l1, m1, r1, out_ref, acc_ref):
    b = pl.program_id(0)
    l = pl.program_id(1)
    blocks = pl.num_programs(0)

    @pl.when(l == 0)
    def _():
        acc_ref[...] = jnp.zeros_like(acc_ref)

    cnt = cnt_ref[l, b]
    for s, (lf, md, rt) in enumerate(((l0, m0, r0), (l1, m1, r1))):
        w = src_ref[l, b, s]
        live = s < cnt
        for ref, cond in ((lf, w < EDGE), (md, (w >= EDGE) & (w < EDGE + blocks)), (rt, w >= EDGE + blocks)):
            @pl.when(live & cond)
            def _():
                acc_ref[...] += jnp.dot(a_ref[s], ref[...], preferred_element_type=jnp.float32)

    @pl.when(l == pl.num_programs(1) - 1)
    def _():
        out_ref[...] = acc_ref[...].astype(out_ref.dtype)


def lag_partial(history, left, right, lag_blocks, pattern, live_counts):
    lags, blocks, vec, ex = history.shape
    slots = lag_blocks.shape[2]
    window = jnp.arange(blocks, dtype=jnp.int32)[None, :, None] + pattern

    def used(src, cnt, l, b, s, lo, hi):
        w = src[l, b, s]
        return (s < cnt[l, b]) & (w >= lo) & (w < hi), w - lo

    def source_spec(s, lo, hi, count):
        def index(b, l, src, cnt):
            on, at = used(src, cnt, l, b, s, lo, hi)
            return (jnp.where(on, l, 0), jnp.where(on, jnp.clip(at, 0, count - 1), 0), 0, 0)
        return pl.BlockSpec((None, None, vec, ex), index)

    def local_spec(s):
        return source_spec(s, EDGE, EDGE + blocks, blocks)

    def left_spec(s):
        return source_spec(s, 0, EDGE, EDGE)

    def right_spec(s):
        return source_spec(s, EDGE + blocks, 2 * EDGE + blocks, EDGE)

    in_specs = [pl.BlockSpec((None, None, slots, vec, vec), lambda b, l, src, cnt: (l, b, 0, 0, 0))]
    operands = [lag_blocks]
    for s in range(slots):
        in_specs += [left_spec(s), local_spec(s), right_spec(s)]
        operands += [left, history, right]
    grid_spec = pltpu.PrefetchScalarGridSpec(
        num_scalar_prefetch=2,
        grid=(blocks, lags),
        in_specs=in_specs,
        out_specs=pl.BlockSpec((None, vec, ex), lambda b, l, src, cnt: (b, 0, 0)),
        scratch_shapes=[pltpu.VMEM((vec, ex), jnp.float32)],
    )
    flops = 2 * lags * blocks * slots * vec * vec * ex
    moved = 2 * (lag_blocks.size + slots * history.size + blocks * vec * ex)
    return pl.pallas_call(
        term_kernel,
        grid_spec=grid_spec,
        out_shape=jax.ShapeDtypeStruct((blocks, vec, ex), jnp.bfloat16),
        cost_estimate=pl.CostEstimate(flops=flops, transcendentals=0, bytes_accessed=moved),
    )(window, live_counts, *operands)


def shifted_by(array, axis, by):
    count = lax.axis_size(axis)
    return lax.ppermute(array, axis, [(i, (i + by) % count) for i in range(count)])


def passed_along(array, axis, by):
    length = lax.axis_size(axis)
    pairs = [(i, i + by) for i in range(length) if 0 <= i + by < length]
    return lax.ppermute(array, axis, pairs)


def shards(history, lag_blocks, self_inverse, excitation, pattern, live_counts):
    blocks_here = history.shape[1]
    half = blocks_here // 2
    early = passed_along(history[-1, :half], "lag", 1)
    left = shifted_by(history[:, blocks_here - EDGE:], "tile", 1)
    right = shifted_by(history[:, :EDGE], "tile", -1)
    oldest, left, right, early = lax.optimization_barrier((history[-1, half:], left, right, early))
    late = passed_along(oldest, "lag", 1)
    live = jnp.minimum(live_counts, lag_blocks.shape[2])
    partial = lag_partial(history, left, right, lag_blocks, pattern, live)

    n_lag = lax.axis_size("lag")
    me = lax.axis_index("lag")
    field = lax.dynamic_index_in_dim(partial, me, 0, keepdims=False).astype(jnp.float32)
    for k in range(1, n_lag):
        piece = lax.dynamic_index_in_dim(partial, (me + k) % n_lag, 0, keepdims=False)
        field = field + shifted_by(piece, "lag", k).astype(jnp.float32)
    mine = lax.dynamic_index_in_dim(excitation, me, 0, keepdims=False)
    residual = (mine - field).astype(jnp.bfloat16)
    inverse = lax.dynamic_index_in_dim(self_inverse, me, 0, keepdims=False)
    block = jnp.dot(inverse, residual, preferred_element_type=jnp.float32).astype(jnp.bfloat16)
    block, late = lax.optimization_barrier((block, late))
    carried = jnp.concatenate([early, late], axis=0)

    gathered = [block] + [shifted_by(block, "lag", k) for k in range(1, n_lag)]
    ordered = jnp.stack(gathered[::-1])
    traction = jnp.roll(ordered, me + 1, axis=0)

    newest = jnp.where(me == 0, traction, carried)
    shifted_history = jnp.concatenate([newest[None], history[:-1]], axis=0)
    return (traction, shifted_history)


def solution(mesh):
    in_specs = (
        P("lag", "tile", None, None),
        P("lag", "tile", None, None, None),
        P("tile", None, None),
        P("tile", None, None),
        P("lag", "tile", None),
        P("lag", "tile"),
    )
    out_specs = (P("tile", None, None), P("lag", "tile", None, None))
    return jax.shard_map(shards, mesh=mesh, in_specs=in_specs, out_specs=out_specs, check_vma=False)
```

```python
import jax
import jax.numpy as jnp
from jax import lax
from jax.experimental import pallas as pl
from jax.experimental.pallas import tpu as pltpu
from jax.sharding import PartitionSpec as P

EDGE = 4


def term_kernel(src_ref, cnt_ref, off_ref, a_ref, l0, m0, r0, l1, m1, r1, out_ref, acc_ref):
    b = pl.program_id(0)
    l = pl.program_id(1)
    blocks = pl.num_programs(0)

    @pl.when(l == 0)
    def _():
        acc_ref[...] = jnp.zeros_like(acc_ref)

    cnt = cnt_ref[l, b]
    for s, (lf, md, rt) in enumerate(((l0, m0, r0), (l1, m1, r1))):
        w = src_ref[l, b, s]
        live = s < cnt
        for ref, cond in ((lf, w < EDGE), (md, (w >= EDGE) & (w < EDGE + blocks)), (rt, w >= EDGE + blocks)):
            @pl.when(live & cond)
            def _():
                acc_ref[...] += jnp.dot(a_ref[s], ref[...], preferred_element_type=jnp.float32)

    @pl.when(l == pl.num_programs(1) - 1)
    def _():
        out_ref[...] = acc_ref[...].astype(out_ref.dtype)


def lag_partial(history, left, right, lag_blocks, pattern, live_counts, offset):
    lags, blocks, vec, ex = history.shape
    slots = lag_blocks.shape[2]
    window = jnp.arange(blocks, dtype=jnp.int32)[None, :, None] + pattern

    def used(src, cnt, l, b, s, lo, hi):
        w = src[l, b, s]
        return (s < cnt[l, b]) & (w >= lo) & (w < hi), w - lo

    def source_spec(s, lo, hi, count):
        def index(b, l, src, cnt, off):
            on, at = used(src, cnt, l, b, s, lo, hi)
            return (jnp.where(on, l, 0), jnp.where(on, jnp.clip(at, 0, count - 1), 0), 0, 0)
        return pl.BlockSpec((None, None, vec, ex), index)

    def local_spec(s):
        return source_spec(s, EDGE, EDGE + blocks, blocks)

    def left_spec(s):
        return source_spec(s, 0, EDGE, EDGE)

    def right_spec(s):
        return source_spec(s, EDGE + blocks, 2 * EDGE + blocks, EDGE)

    in_specs = [pl.BlockSpec((None, None, slots, vec, vec), lambda b, l, src, cnt, off: (l, b, 0, 0, 0))]
    operands = [lag_blocks]
    for s in range(slots):
        in_specs += [left_spec(s), local_spec(s), right_spec(s)]
        operands += [left, history, right]
    grid_spec = pltpu.PrefetchScalarGridSpec(
        num_scalar_prefetch=3,
        grid=(blocks, lags),
        in_specs=in_specs,
        out_specs=pl.BlockSpec((None, vec, ex), lambda b, l, src, cnt, off: ((b - off[0]) % blocks, 0, 0)),
        scratch_shapes=[pltpu.VMEM((vec, ex), jnp.float32)],
    )
    flops = 2 * lags * blocks * slots * vec * vec * ex
    moved = 2 * (lag_blocks.size + slots * history.size + blocks * vec * ex)
    return pl.pallas_call(
        term_kernel,
        grid_spec=grid_spec,
        out_shape=jax.ShapeDtypeStruct((blocks, vec, ex), jnp.bfloat16),
        cost_estimate=pl.CostEstimate(flops=flops, transcendentals=0, bytes_accessed=moved),
    )(window, live_counts, offset, *operands)


def shifted_by(array, axis, by):
    count = lax.axis_size(axis)
    return lax.ppermute(array, axis, [(i, (i + by) % count) for i in range(count)])


def passed_along(array, axis, by):
    length = lax.axis_size(axis)
    pairs = [(i, i + by) for i in range(length) if 0 <= i + by < length]
    return lax.ppermute(array, axis, pairs)


def shards(history, lag_blocks, self_inverse, excitation, pattern, live_counts):
    blocks_here = history.shape[1]
    half = blocks_here // 2
    early = passed_along(history[-1, :half], "lag", 1)
    left = shifted_by(history[:, blocks_here - EDGE:], "tile", 1)
    right = shifted_by(history[:, :EDGE], "tile", -1)
    oldest, left, right, early = lax.optimization_barrier((history[-1, half:], left, right, early))
    late = passed_along(oldest, "lag", 1)
    live = jnp.minimum(live_counts, lag_blocks.shape[2])
    n_lag = lax.axis_size("lag")
    me = lax.axis_index("lag")
    offset = jnp.full((1,), me, jnp.int32)
    partial = lag_partial(history, left, right, lag_blocks, pattern, live, offset)

    field = partial[0].astype(jnp.float32)
    for k in range(1, n_lag):
        field = field + shifted_by(partial[k], "lag", k).astype(jnp.float32)
    mine = lax.dynamic_index_in_dim(excitation, me, 0, keepdims=False)
    residual = (mine - field).astype(jnp.bfloat16)
    inverse = lax.dynamic_index_in_dim(self_inverse, me, 0, keepdims=False)
    block = jnp.dot(inverse, residual, preferred_element_type=jnp.float32).astype(jnp.bfloat16)
    block, late = lax.optimization_barrier((block, late))
    carried = jnp.concatenate([early, late], axis=0)
    shifted_history = jnp.concatenate([carried[None], history[:-1]], axis=0)

    gathered = [block] + [shifted_by(block, "lag", k) for k in range(1, n_lag)]
    ordered = jnp.stack(gathered[::-1])
    traction = jnp.roll(ordered, me + 1, axis=0)

    newest = jnp.where(me == 0, traction, carried)
    shifted_history = lax.dynamic_update_slice(shifted_history, newest[None], (0, 0, 0, 0))
    return (traction, shifted_history)


def solution(mesh):
    in_specs = (
        P("lag", "tile", None, None),
        P("lag", "tile", None, None, None),
        P("tile", None, None),
        P("tile", None, None),
        P("lag", "tile", None),
        P("lag", "tile"),
    )
    out_specs = (P("tile", None, None), P("lag", "tile", None, None))
    return jax.shard_map(shards, mesh=mesh, in_specs=in_specs, out_specs=out_specs, check_vma=False)
```

```python
import jax
import jax.numpy as jnp
from jax import lax
from jax.experimental import pallas as pl
from jax.experimental.pallas import tpu as pltpu
from jax.sharding import PartitionSpec as P

EDGE = 4


def term_kernel(src_ref, cnt_ref, a_ref, l0, m0, r0, l1, m1, r1, out_ref, acc_ref):
    b = pl.program_id(0)
    l = pl.program_id(1)
    blocks = pl.num_programs(0)

    @pl.when(l == 0)
    def _():
        acc_ref[...] = jnp.zeros_like(acc_ref)

    cnt = cnt_ref[l, b]
    for s, (lf, md, rt) in enumerate(((l0, m0, r0), (l1, m1, r1))):
        w = src_ref[l, b, s]
        live = s < cnt
        for ref, cond in ((lf, w < EDGE), (md, (w >= EDGE) & (w < EDGE + blocks)), (rt, w >= EDGE + blocks)):
            @pl.when(live & cond)
            def _():
                acc_ref[...] += jnp.dot(a_ref[s], ref[...], preferred_element_type=jnp.float32)

    @pl.when(l == pl.num_programs(1) - 1)
    def _():
        out_ref[...] = acc_ref[...].astype(out_ref.dtype)


def lag_partial(history, left, right, lag_blocks, pattern, live_counts):
    lags, blocks, vec, ex = history.shape
    slots = lag_blocks.shape[2]
    window = jnp.arange(blocks, dtype=jnp.int32)[None, :, None] + pattern

    def used(src, cnt, l, b, s, lo, hi):
        w = src[l, b, s]
        return (s < cnt[l, b]) & (w >= lo) & (w < hi), w - lo

    def source_spec(s, lo, hi, count):
        def index(b, l, src, cnt):
            on, at = used(src, cnt, l, b, s, lo, hi)
            return (jnp.where(on, l, 0), jnp.where(on, jnp.clip(at, 0, count - 1), 0), 0, 0)
        return pl.BlockSpec((None, None, vec, ex), index)

    def local_spec(s):
        return source_spec(s, EDGE, EDGE + blocks, blocks)

    def left_spec(s):
        return source_spec(s, 0, EDGE, EDGE)

    def right_spec(s):
        return source_spec(s, EDGE + blocks, 2 * EDGE + blocks, EDGE)

    in_specs = [pl.BlockSpec((None, None, slots, vec, vec), lambda b, l, src, cnt: (l, b, 0, 0, 0))]
    operands = [lag_blocks]
    for s in range(slots):
        in_specs += [left_spec(s), local_spec(s), right_spec(s)]
        operands += [left, history, right]
    grid_spec = pltpu.PrefetchScalarGridSpec(
        num_scalar_prefetch=2,
        grid=(blocks, lags),
        in_specs=in_specs,
        out_specs=pl.BlockSpec((None, vec, ex), lambda b, l, src, cnt: (b, 0, 0)),
        scratch_shapes=[pltpu.VMEM((vec, ex), jnp.float32)],
    )
    flops = 2 * lags * blocks * slots * vec * vec * ex
    moved = 2 * (lag_blocks.size + slots * history.size + blocks * vec * ex)
    return pl.pallas_call(
        term_kernel,
        grid_spec=grid_spec,
        out_shape=jax.ShapeDtypeStruct((blocks, vec, ex), jnp.bfloat16),
        cost_estimate=pl.CostEstimate(flops=flops, transcendentals=0, bytes_accessed=moved),
    )(window, live_counts, *operands)


def shifted_by(array, axis, by):
    count = lax.axis_size(axis)
    return lax.ppermute(array, axis, [(i, (i + by) % count) for i in range(count)])


def passed_along(array, axis, by):
    length = lax.axis_size(axis)
    pairs = [(i, i + by) for i in range(length) if 0 <= i + by < length]
    return lax.ppermute(array, axis, pairs)


def shards(history, lag_blocks, self_inverse, excitation, pattern, live_counts):
    blocks_here = history.shape[1]
    half = blocks_here // 2
    early = passed_along(history[-1, :half], "lag", 1)
    left = shifted_by(history[:, blocks_here - EDGE:], "tile", 1)
    right = shifted_by(history[:, :EDGE], "tile", -1)
    oldest, left, right, early = lax.optimization_barrier((history[-1, half:], left, right, early))
    late = passed_along(oldest, "lag", 1)
    live = jnp.minimum(live_counts, lag_blocks.shape[2])
    partial = lag_partial(history, left, right, lag_blocks, pattern, live)

    n_lag = lax.axis_size("lag")
    me = lax.axis_index("lag")
    received = lax.all_to_all(partial, "lag", 0, 0, tiled=True)
    field = jnp.sum(received.astype(jnp.float32), axis=0)
    mine = lax.dynamic_index_in_dim(excitation, me, 0, keepdims=False)
    residual = (mine - field).astype(jnp.bfloat16)
    inverse = lax.dynamic_index_in_dim(self_inverse, me, 0, keepdims=False)
    block = jnp.dot(inverse, residual, preferred_element_type=jnp.float32).astype(jnp.bfloat16)
    block, late = lax.optimization_barrier((block, late))
    carried = jnp.concatenate([early, late], axis=0)

    gathered = [block] + [shifted_by(block, "lag", k) for k in range(1, n_lag)]
    ordered = jnp.stack(gathered[::-1])
    traction = jnp.roll(ordered, me + 1, axis=0)

    newest = jnp.where(me == 0, traction, carried)
    shifted_history = jnp.concatenate([newest[None], history[:-1]], axis=0)
    return (traction, shifted_history)


def solution(mesh):
    in_specs = (
        P("lag", "tile", None, None),
        P("lag", "tile", None, None, None),
        P("tile", None, None),
        P("tile", None, None),
        P("lag", "tile", None),
        P("lag", "tile"),
    )
    out_specs = (P("tile", None, None), P("lag", "tile", None, None))
    return jax.shard_map(shards, mesh=mesh, in_specs=in_specs, out_specs=out_specs, check_vma=False)
```

```python
import jax
import jax.numpy as jnp
from jax import lax
from jax.experimental import pallas as pl
from jax.experimental.pallas import tpu as pltpu
from jax.sharding import PartitionSpec as P

EDGE = 4


def term_kernel(src_ref, cnt_ref, a_ref, l0, m0, r0, l1, m1, r1, out_ref, acc_ref):
    b = pl.program_id(0)
    l = pl.program_id(1)
    blocks = pl.num_programs(0)

    @pl.when(l == 0)
    def _():
        acc_ref[...] = jnp.zeros_like(acc_ref)

    cnt = cnt_ref[l, b]
    for s, (lf, md, rt) in enumerate(((l0, m0, r0), (l1, m1, r1))):
        w = src_ref[l, b, s]
        live = s < cnt
        for ref, cond in ((lf, w < EDGE), (md, (w >= EDGE) & (w < EDGE + blocks)), (rt, w >= EDGE + blocks)):
            @pl.when(live & cond)
            def _():
                acc_ref[...] += jnp.dot(a_ref[s], ref[...], preferred_element_type=jnp.float32)

    @pl.when(l == pl.num_programs(1) - 1)
    def _():
        out_ref[...] = acc_ref[...].astype(out_ref.dtype)


def lag_partial(history, left, right, lag_blocks, pattern, live_counts):
    lags, blocks, vec, ex = history.shape
    slots = lag_blocks.shape[2]
    window = jnp.arange(blocks, dtype=jnp.int32)[None, :, None] + pattern

    def used(src, cnt, l, b, s, lo, hi):
        w = src[l, b, s]
        return (s < cnt[l, b]) & (w >= lo) & (w < hi), w - lo

    def source_spec(s, lo, hi, count):
        def index(b, l, src, cnt):
            on, at = used(src, cnt, l, b, s, lo, hi)
            return (jnp.where(on, l, 0), jnp.where(on, jnp.clip(at, 0, count - 1), 0), 0, 0)
        return pl.BlockSpec((None, None, vec, ex), index)

    def local_spec(s):
        return source_spec(s, EDGE, EDGE + blocks, blocks)

    def left_spec(s):
        return source_spec(s, 0, EDGE, EDGE)

    def right_spec(s):
        return source_spec(s, EDGE + blocks, 2 * EDGE + blocks, EDGE)

    in_specs = [pl.BlockSpec((None, None, slots, vec, vec), lambda b, l, src, cnt: (l, b, 0, 0, 0))]
    operands = [lag_blocks]
    for s in range(slots):
        in_specs += [left_spec(s), local_spec(s), right_spec(s)]
        operands += [left, history, right]
    grid_spec = pltpu.PrefetchScalarGridSpec(
        num_scalar_prefetch=2,
        grid=(blocks, lags),
        in_specs=in_specs,
        out_specs=pl.BlockSpec((None, vec, ex), lambda b, l, src, cnt: (b, 0, 0)),
        scratch_shapes=[pltpu.VMEM((vec, ex), jnp.float32)],
    )
    flops = 2 * lags * blocks * slots * vec * vec * ex
    moved = 2 * (lag_blocks.size + slots * history.size + blocks * vec * ex)
    return pl.pallas_call(
        term_kernel,
        grid_spec=grid_spec,
        out_shape=jax.ShapeDtypeStruct((blocks, vec, ex), jnp.bfloat16),
        cost_estimate=pl.CostEstimate(flops=flops, transcendentals=0, bytes_accessed=moved),
    )(window, live_counts, *operands)


def shifted_by(array, axis, by):
    count = lax.axis_size(axis)
    return lax.ppermute(array, axis, [(i, (i + by) % count) for i in range(count)])


def passed_along(array, axis, by):
    length = lax.axis_size(axis)
    pairs = [(i, i + by) for i in range(length) if 0 <= i + by < length]
    return lax.ppermute(array, axis, pairs)


def shards(history, lag_blocks, self_inverse, excitation, pattern, live_counts):
    blocks_here = history.shape[1]
    half = blocks_here // 2
    early = passed_along(history[-1, :half], "lag", 1)
    left = shifted_by(history[:, blocks_here - EDGE:], "tile", 1)
    right = shifted_by(history[:, :EDGE], "tile", -1)
    oldest, left, right, early = lax.optimization_barrier((history[-1, half:], left, right, early))
    late = passed_along(oldest, "lag", 1)
    live = jnp.minimum(live_counts, lag_blocks.shape[2])
    partial = lag_partial(history, left, right, lag_blocks, pattern, live)
    partial, late = lax.optimization_barrier((partial, late))

    n_lag = lax.axis_size("lag")
    me = lax.axis_index("lag")
    field = lax.dynamic_index_in_dim(partial, me, 0, keepdims=False).astype(jnp.float32)
    for k in range(1, n_lag):
        piece = lax.dynamic_index_in_dim(partial, (me + k) % n_lag, 0, keepdims=False)
        field = field + shifted_by(piece, "lag", k).astype(jnp.float32)
    mine = lax.dynamic_index_in_dim(excitation, me, 0, keepdims=False)
    residual = (mine - field).astype(jnp.bfloat16)
    inverse = lax.dynamic_index_in_dim(self_inverse, me, 0, keepdims=False)
    block = jnp.dot(inverse, residual, preferred_element_type=jnp.float32).astype(jnp.bfloat16)
    carried = jnp.concatenate([early, late], axis=0)

    gathered = [block] + [shifted_by(block, "lag", k) for k in range(1, n_lag)]
    ordered = jnp.stack(gathered[::-1])
    traction = jnp.roll(ordered, me + 1, axis=0)

    newest = jnp.where(me == 0, traction, carried)
    shifted_history = jnp.concatenate([newest[None], history[:-1]], axis=0)
    return (traction, shifted_history)


def solution(mesh):
    in_specs = (
        P("lag", "tile", None, None),
        P("lag", "tile", None, None, None),
        P("tile", None, None),
        P("tile", None, None),
        P("lag", "tile", None),
        P("lag", "tile"),
    )
    out_specs = (P("tile", None, None), P("lag", "tile", None, None))
    return jax.shard_map(shards, mesh=mesh, in_specs=in_specs, out_specs=out_specs, check_vma=False)
```

```python
import jax
import jax.numpy as jnp
from jax import lax
from jax.experimental import pallas as pl
from jax.experimental.pallas import tpu as pltpu
from jax.sharding import PartitionSpec as P

EDGE = 4


def term_kernel(src_ref, cnt_ref, off_ref, a_ref, l0, m0, r0, l1, m1, r1, out_ref, acc_ref):
    b = pl.program_id(0)
    l = pl.program_id(1)
    blocks = pl.num_programs(0)

    @pl.when(l == 0)
    def _():
        acc_ref[...] = jnp.zeros_like(acc_ref)

    cnt = cnt_ref[l, b]
    for s, (lf, md, rt) in enumerate(((l0, m0, r0), (l1, m1, r1))):
        w = src_ref[l, b, s]
        live = s < cnt
        for ref, cond in ((lf, w < EDGE), (md, (w >= EDGE) & (w < EDGE + blocks)), (rt, w >= EDGE + blocks)):
            @pl.when(live & cond)
            def _():
                acc_ref[...] += jnp.dot(a_ref[s], ref[...], preferred_element_type=jnp.float32)

    @pl.when(l == pl.num_programs(1) - 1)
    def _():
        out_ref[...] = acc_ref[...].astype(out_ref.dtype)


def lag_partial(history, left, right, lag_blocks, pattern, live_counts, offset):
    lags, blocks, vec, ex = history.shape
    slots = lag_blocks.shape[2]
    window = jnp.arange(blocks, dtype=jnp.int32)[None, :, None] + pattern

    def used(src, cnt, l, b, s, lo, hi):
        w = src[l, b, s]
        return (s < cnt[l, b]) & (w >= lo) & (w < hi), w - lo

    def source_spec(s, lo, hi, count):
        def index(b, l, src, cnt, off):
            on, at = used(src, cnt, l, b, s, lo, hi)
            return (jnp.where(on, l, 0), jnp.where(on, jnp.clip(at, 0, count - 1), 0), 0, 0)
        return pl.BlockSpec((None, None, vec, ex), index)

    def local_spec(s):
        return source_spec(s, EDGE, EDGE + blocks, blocks)

    def left_spec(s):
        return source_spec(s, 0, EDGE, EDGE)

    def right_spec(s):
        return source_spec(s, EDGE + blocks, 2 * EDGE + blocks, EDGE)

    in_specs = [pl.BlockSpec((None, None, slots, vec, vec), lambda b, l, src, cnt, off: (l, b, 0, 0, 0))]
    operands = [lag_blocks]
    for s in range(slots):
        in_specs += [left_spec(s), local_spec(s), right_spec(s)]
        operands += [left, history, right]
    grid_spec = pltpu.PrefetchScalarGridSpec(
        num_scalar_prefetch=3,
        grid=(blocks, lags),
        in_specs=in_specs,
        out_specs=pl.BlockSpec((None, vec, ex), lambda b, l, src, cnt, off: ((b - off[0]) % blocks, 0, 0)),
        scratch_shapes=[pltpu.VMEM((vec, ex), jnp.float32)],
    )
    flops = 2 * lags * blocks * slots * vec * vec * ex
    moved = 2 * (lag_blocks.size + slots * history.size + blocks * vec * ex)
    return pl.pallas_call(
        term_kernel,
        grid_spec=grid_spec,
        out_shape=jax.ShapeDtypeStruct((blocks, vec, ex), jnp.bfloat16),
        cost_estimate=pl.CostEstimate(flops=flops, transcendentals=0, bytes_accessed=moved),
    )(window, live_counts, offset, *operands)


def shifted_by(array, axis, by):
    count = lax.axis_size(axis)
    return lax.ppermute(array, axis, [(i, (i + by) % count) for i in range(count)])


def passed_along(array, axis, by):
    length = lax.axis_size(axis)
    pairs = [(i, i + by) for i in range(length) if 0 <= i + by < length]
    return lax.ppermute(array, axis, pairs)


def shards(history, lag_blocks, self_inverse, excitation, pattern, live_counts):
    blocks_here = history.shape[1]
    half = blocks_here // 2
    early = passed_along(history[-1, :half], "lag", 1)
    left = shifted_by(history[:, blocks_here - EDGE:], "tile", 1)
    right = shifted_by(history[:, :EDGE], "tile", -1)
    oldest, left, right, early = lax.optimization_barrier((history[-1, half:], left, right, early))
    late = passed_along(oldest, "lag", 1)
    live = jnp.minimum(live_counts, lag_blocks.shape[2])
    n_lag = lax.axis_size("lag")
    me = lax.axis_index("lag")
    offset = jnp.full((1,), me, jnp.int32)
    partial = lag_partial(history, left, right, lag_blocks, pattern, live, offset)

    field = partial[0].astype(jnp.float32)
    for k in range(1, n_lag):
        field = field + shifted_by(partial[k], "lag", k).astype(jnp.float32)
    mine = lax.dynamic_index_in_dim(excitation, me, 0, keepdims=False)
    residual = (mine - field).astype(jnp.bfloat16)
    inverse = lax.dynamic_index_in_dim(self_inverse, me, 0, keepdims=False)
    block = jnp.dot(inverse, residual, preferred_element_type=jnp.float32).astype(jnp.bfloat16)
    block, late = lax.optimization_barrier((block, late))
    carried = jnp.concatenate([early, late], axis=0)

    gathered = [block] + [shifted_by(block, "lag", k) for k in range(1, n_lag)]
    ordered = jnp.stack(gathered[::-1])
    traction = jnp.roll(ordered, me + 1, axis=0)

    newest = jnp.where(me == 0, traction, carried)
    shifted_history = jnp.concatenate([newest[None], history[:-1]], axis=0)
    return (traction, shifted_history)


def solution(mesh):
    in_specs = (
        P("lag", "tile", None, None),
        P("lag", "tile", None, None, None),
        P("tile", None, None),
        P("tile", None, None),
        P("lag", "tile", None),
        P("lag", "tile"),
    )
    out_specs = (P("tile", None, None), P("lag", "tile", None, None))
    return jax.shard_map(shards, mesh=mesh, in_specs=in_specs, out_specs=out_specs, check_vma=False)
```

```python
import jax
import jax.numpy as jnp
from jax import lax
from jax.experimental import pallas as pl
from jax.experimental.pallas import tpu as pltpu
from jax.sharding import PartitionSpec as P

EDGE = 4


def term_kernel(src_ref, cnt_ref, a_ref, l0, m0, r0, l1, m1, r1, out_ref, acc_ref):
    b = pl.program_id(0)
    l = pl.program_id(1)
    blocks = pl.num_programs(0)

    @pl.when(l == 0)
    def _():
        acc_ref[...] = jnp.zeros_like(acc_ref)

    cnt = cnt_ref[l, b]
    for s, (lf, md, rt) in enumerate(((l0, m0, r0), (l1, m1, r1))):
        w = src_ref[l, b, s]
        live = s < cnt
        for ref, cond in ((lf, w < EDGE), (md, (w >= EDGE) & (w < EDGE + blocks)), (rt, w >= EDGE + blocks)):
            @pl.when(live & cond)
            def _():
                acc_ref[...] += jnp.dot(a_ref[s], ref[...], preferred_element_type=jnp.float32)

    @pl.when(l == pl.num_programs(1) - 1)
    def _():
        out_ref[...] = acc_ref[...].astype(out_ref.dtype)


def lag_partial(history, left, right, lag_blocks, pattern, live_counts):
    lags, blocks, vec, ex = history.shape
    slots = lag_blocks.shape[2]
    window = jnp.arange(blocks, dtype=jnp.int32)[None, :, None] + pattern

    def used(src, cnt, l, b, s, lo, hi):
        w = src[l, b, s]
        return (s < cnt[l, b]) & (w >= lo) & (w < hi), w - lo

    def source_spec(s, lo, hi, count):
        def index(b, l, src, cnt):
            on, at = used(src, cnt, l, b, s, lo, hi)
            return (jnp.where(on, l, 0), jnp.where(on, jnp.clip(at, 0, count - 1), 0), 0, 0)
        return pl.BlockSpec((None, None, vec, ex), index)

    def local_spec(s):
        return source_spec(s, EDGE, EDGE + blocks, blocks)

    def left_spec(s):
        return source_spec(s, 0, EDGE, EDGE)

    def right_spec(s):
        return source_spec(s, EDGE + blocks, 2 * EDGE + blocks, EDGE)

    in_specs = [pl.BlockSpec((None, None, slots, vec, vec), lambda b, l, src, cnt: (l, b, 0, 0, 0))]
    operands = [lag_blocks]
    for s in range(slots):
        in_specs += [left_spec(s), local_spec(s), right_spec(s)]
        operands += [left, history, right]
    grid_spec = pltpu.PrefetchScalarGridSpec(
        num_scalar_prefetch=2,
        grid=(blocks, lags),
        in_specs=in_specs,
        out_specs=pl.BlockSpec((None, vec, ex), lambda b, l, src, cnt: (b, 0, 0)),
        scratch_shapes=[pltpu.VMEM((vec, ex), jnp.float32)],
    )
    flops = 2 * lags * blocks * slots * vec * vec * ex
    moved = 2 * (lag_blocks.size + slots * history.size + blocks * vec * ex)
    return pl.pallas_call(
        term_kernel,
        grid_spec=grid_spec,
        out_shape=jax.ShapeDtypeStruct((blocks, vec, ex), jnp.bfloat16),
        cost_estimate=pl.CostEstimate(flops=flops, transcendentals=0, bytes_accessed=moved),
    )(window, live_counts, *operands)


def shifted_by(array, axis, by):
    count = lax.axis_size(axis)
    return lax.ppermute(array, axis, [(i, (i + by) % count) for i in range(count)])


def passed_along(array, axis, by):
    length = lax.axis_size(axis)
    pairs = [(i, i + by) for i in range(length) if 0 <= i + by < length]
    return lax.ppermute(array, axis, pairs)


def shards(history, lag_blocks, self_inverse, excitation, pattern, live_counts):
    blocks_here = history.shape[1]
    half = blocks_here // 2
    early = passed_along(history[-1, :half], "lag", 1)
    left = shifted_by(history[:, blocks_here - EDGE:], "tile", 1)
    right = shifted_by(history[:, :EDGE], "tile", -1)
    after, left, right, early = lax.optimization_barrier((history, left, right, early))
    late = passed_along(after[-1, half:], "lag", 1)
    live = jnp.minimum(live_counts, lag_blocks.shape[2])
    partial = lag_partial(history, left, right, lag_blocks, pattern, live)

    n_lag = lax.axis_size("lag")
    me = lax.axis_index("lag")
    field = lax.dynamic_index_in_dim(partial, me, 0, keepdims=False).astype(jnp.float32)
    for k in range(1, n_lag):
        piece = lax.dynamic_index_in_dim(partial, (me + k) % n_lag, 0, keepdims=False)
        field = field + shifted_by(piece, "lag", k).astype(jnp.float32)
    mine = lax.dynamic_index_in_dim(excitation, me, 0, keepdims=False)
    residual = (mine - field).astype(jnp.bfloat16)
    inverse = lax.dynamic_index_in_dim(self_inverse, me, 0, keepdims=False)
    block = jnp.dot(inverse, residual, preferred_element_type=jnp.float32).astype(jnp.bfloat16)
    block, late = lax.optimization_barrier((block, late))
    carried = jnp.concatenate([early, late], axis=0)

    gathered = [block] + [shifted_by(block, "lag", k) for k in range(1, n_lag)]
    ordered = jnp.stack(gathered[::-1])
    traction = jnp.roll(ordered, me + 1, axis=0)

    newest = jnp.where(me == 0, traction, carried)
    shifted_history = jnp.concatenate([newest[None], history[:-1]], axis=0)
    return (traction, shifted_history)


def solution(mesh):
    in_specs = (
        P("lag", "tile", None, None),
        P("lag", "tile", None, None, None),
        P("tile", None, None),
        P("tile", None, None),
        P("lag", "tile", None),
        P("lag", "tile"),
    )
    out_specs = (P("tile", None, None), P("lag", "tile", None, None))
    return jax.shard_map(shards, mesh=mesh, in_specs=in_specs, out_specs=out_specs, check_vma=False)
```

```python
import jax
import jax.numpy as jnp
from jax import lax
from jax.experimental import pallas as pl
from jax.experimental.pallas import tpu as pltpu
from jax.sharding import PartitionSpec as P

EDGE = 4


def term_kernel(src_ref, cnt_ref, a_ref, *refs):
    *sources, out_ref, acc_ref = refs
    b = pl.program_id(0)
    blocks = pl.num_programs(0)
    lags, slots = a_ref.shape[0], a_ref.shape[1]
    acc_ref[...] = jnp.zeros_like(acc_ref)
    for l in range(lags):
        cnt = cnt_ref[l, b]
        for s in range(slots):
            lf, md, rt = sources[3 * (l * slots + s):3 * (l * slots + s) + 3]
            w = src_ref[l, b, s]
            live = s < cnt
            for ref, cond in ((lf, w < EDGE), (md, (w >= EDGE) & (w < EDGE + blocks)), (rt, w >= EDGE + blocks)):
                @pl.when(live & cond)
                def _():
                    acc_ref[...] += jnp.dot(a_ref[l, s], ref[...], preferred_element_type=jnp.float32)
    out_ref[...] = acc_ref[...].astype(out_ref.dtype)


def lag_partial(history, left, right, lag_blocks, pattern, live_counts):
    lags, blocks, vec, ex = history.shape
    slots = lag_blocks.shape[2]
    window = jnp.arange(blocks, dtype=jnp.int32)[None, :, None] + pattern

    def source_spec(l, s, lo, hi, count):
        def index(b, src, cnt):
            w = src[l, b, s]
            on = (s < cnt[l, b]) & (w >= lo) & (w < hi)
            return (jnp.where(on, l, 0), jnp.where(on, jnp.clip(w - lo, 0, count - 1), 0), 0, 0)
        return pl.BlockSpec((None, None, vec, ex), index)

    in_specs = [pl.BlockSpec((lags, None, slots, vec, vec), lambda b, src, cnt: (0, b, 0, 0, 0))]
    operands = [lag_blocks]
    for l in range(lags):
        for s in range(slots):
            in_specs += [
                source_spec(l, s, 0, EDGE, EDGE),
                source_spec(l, s, EDGE, EDGE + blocks, blocks),
                source_spec(l, s, EDGE + blocks, 2 * EDGE + blocks, EDGE),
            ]
            operands += [left, history, right]
    grid_spec = pltpu.PrefetchScalarGridSpec(
        num_scalar_prefetch=2,
        grid=(blocks,),
        in_specs=in_specs,
        out_specs=pl.BlockSpec((None, vec, ex), lambda b, src, cnt: (b, 0, 0)),
        scratch_shapes=[pltpu.VMEM((vec, ex), jnp.float32)],
    )
    flops = 2 * lags * blocks * slots * vec * vec * ex
    moved = 2 * (lag_blocks.size + slots * history.size + blocks * vec * ex)
    return pl.pallas_call(
        term_kernel,
        grid_spec=grid_spec,
        out_shape=jax.ShapeDtypeStruct((blocks, vec, ex), jnp.bfloat16),
        cost_estimate=pl.CostEstimate(flops=flops, transcendentals=0, bytes_accessed=moved),
    )(window, live_counts, *operands)


def shifted_by(array, axis, by):
    count = lax.axis_size(axis)
    return lax.ppermute(array, axis, [(i, (i + by) % count) for i in range(count)])


def passed_along(array, axis, by):
    length = lax.axis_size(axis)
    pairs = [(i, i + by) for i in range(length) if 0 <= i + by < length]
    return lax.ppermute(array, axis, pairs)


def shards(history, lag_blocks, self_inverse, excitation, pattern, live_counts):
    blocks_here = history.shape[1]
    half = blocks_here // 2
    early = passed_along(history[-1, :half], "lag", 1)
    left = shifted_by(history[:, blocks_here - EDGE:], "tile", 1)
    right = shifted_by(history[:, :EDGE], "tile", -1)
    oldest, left, right, early = lax.optimization_barrier((history[-1, half:], left, right, early))
    late = passed_along(oldest, "lag", 1)
    live = jnp.minimum(live_counts, lag_blocks.shape[2])
    partial = lag_partial(history, left, right, lag_blocks, pattern, live)

    n_lag = lax.axis_size("lag")
    me = lax.axis_index("lag")
    field = lax.dynamic_index_in_dim(partial, me, 0, keepdims=False).astype(jnp.float32)
    for k in range(1, n_lag):
        piece = lax.dynamic_index_in_dim(partial, (me + k) % n_lag, 0, keepdims=False)
        field = field + shifted_by(piece, "lag", k).astype(jnp.float32)
    mine = lax.dynamic_index_in_dim(excitation, me, 0, keepdims=False)
    residual = (mine - field).astype(jnp.bfloat16)
    inverse = lax.dynamic_index_in_dim(self_inverse, me, 0, keepdims=False)
    block = jnp.dot(inverse, residual, preferred_element_type=jnp.float32).astype(jnp.bfloat16)
    block, late = lax.optimization_barrier((block, late))
    carried = jnp.concatenate([early, late], axis=0)

    gathered = [block] + [shifted_by(block, "lag", k) for k in range(1, n_lag)]
    ordered = jnp.stack(gathered[::-1])
    traction = jnp.roll(ordered, me + 1, axis=0)

    newest = jnp.where(me == 0, traction, carried)
    shifted_history = jnp.concatenate([newest[None], history[:-1]], axis=0)
    return (traction, shifted_history)


def solution(mesh):
    in_specs = (
        P("lag", "tile", None, None),
        P("lag", "tile", None, None, None),
        P("tile", None, None),
        P("tile", None, None),
        P("lag", "tile", None),
        P("lag", "tile"),
    )
    out_specs = (P("tile", None, None), P("lag", "tile", None, None))
    return jax.shard_map(shards, mesh=mesh, in_specs=in_specs, out_specs=out_specs, check_vma=False)
```

```python
import jax
import jax.numpy as jnp
from jax import lax
from jax.experimental import pallas as pl
from jax.experimental.pallas import tpu as pltpu
from jax.sharding import PartitionSpec as P

EDGE = 4


def term_kernel(src_ref, cnt_ref, a_ref, left_ref, hist_ref, right_ref, out_ref, acc_ref):
    b = pl.program_id(0)
    lags, slots = a_ref.shape[0], a_ref.shape[1]
    blocks = hist_ref.shape[1]
    acc_ref[...] = jnp.zeros_like(acc_ref)
    for l in range(lags):
        cnt = cnt_ref[l, b]
        for s in range(slots):
            w = src_ref[l, b, s]
            live = s < cnt
            picks = (
                (left_ref, w < EDGE, jnp.clip(w, 0, EDGE - 1)),
                (hist_ref, (w >= EDGE) & (w < EDGE + blocks), jnp.clip(w - EDGE, 0, blocks - 1)),
                (right_ref, w >= EDGE + blocks, jnp.clip(w - EDGE - blocks, 0, EDGE - 1)),
            )
            for ref, cond, at in picks:
                @pl.when(live & cond)
                def _():
                    acc_ref[...] += jnp.dot(a_ref[l, s], ref[l, at], preferred_element_type=jnp.float32)
    out_ref[...] = acc_ref[...].astype(out_ref.dtype)


def lag_partial(history, left, right, lag_blocks, pattern, live_counts):
    lags, blocks, vec, ex = history.shape
    slots = lag_blocks.shape[2]
    window = jnp.arange(blocks, dtype=jnp.int32)[None, :, None] + pattern

    def whole(array):
        return pl.BlockSpec(array.shape, lambda b, src, cnt: (0,) * array.ndim)

    in_specs = [
        pl.BlockSpec((lags, None, slots, vec, vec), lambda b, src, cnt: (0, b, 0, 0, 0)),
        whole(left),
        whole(history),
        whole(right),
    ]
    grid_spec = pltpu.PrefetchScalarGridSpec(
        num_scalar_prefetch=2,
        grid=(blocks,),
        in_specs=in_specs,
        out_specs=pl.BlockSpec((None, vec, ex), lambda b, src, cnt: (b, 0, 0)),
        scratch_shapes=[pltpu.VMEM((vec, ex), jnp.float32)],
    )
    flops = 2 * lags * blocks * slots * vec * vec * ex
    moved = 2 * (lag_blocks.size + history.size + left.size + right.size + blocks * vec * ex)
    return pl.pallas_call(
        term_kernel,
        grid_spec=grid_spec,
        out_shape=jax.ShapeDtypeStruct((blocks, vec, ex), jnp.bfloat16),
        cost_estimate=pl.CostEstimate(flops=flops, transcendentals=0, bytes_accessed=moved),
    )(window, live_counts, lag_blocks, left, history, right)


def shifted_by(array, axis, by):
    count = lax.axis_size(axis)
    return lax.ppermute(array, axis, [(i, (i + by) % count) for i in range(count)])


def passed_along(array, axis, by):
    length = lax.axis_size(axis)
    pairs = [(i, i + by) for i in range(length) if 0 <= i + by < length]
    return lax.ppermute(array, axis, pairs)


def shards(history, lag_blocks, self_inverse, excitation, pattern, live_counts):
    blocks_here = history.shape[1]
    half = blocks_here // 2
    early = passed_along(history[-1, :half], "lag", 1)
    left = shifted_by(history[:, blocks_here - EDGE:], "tile", 1)
    right = shifted_by(history[:, :EDGE], "tile", -1)
    oldest, left, right, early = lax.optimization_barrier((history[-1, half:], left, right, early))
    late = passed_along(oldest, "lag", 1)
    live = jnp.minimum(live_counts, lag_blocks.shape[2])
    partial = lag_partial(history, left, right, lag_blocks, pattern, live)

    n_lag = lax.axis_size("lag")
    me = lax.axis_index("lag")
    field = lax.dynamic_index_in_dim(partial, me, 0, keepdims=False).astype(jnp.float32)
    for k in range(1, n_lag):
        piece = lax.dynamic_index_in_dim(partial, (me + k) % n_lag, 0, keepdims=False)
        field = field + shifted_by(piece, "lag", k).astype(jnp.float32)
    mine = lax.dynamic_index_in_dim(excitation, me, 0, keepdims=False)
    residual = (mine - field).astype(jnp.bfloat16)
    inverse = lax.dynamic_index_in_dim(self_inverse, me, 0, keepdims=False)
    block = jnp.dot(inverse, residual, preferred_element_type=jnp.float32).astype(jnp.bfloat16)
    block, late = lax.optimization_barrier((block, late))
    carried = jnp.concatenate([early, late], axis=0)

    gathered = [block] + [shifted_by(block, "lag", k) for k in range(1, n_lag)]
    ordered = jnp.stack(gathered[::-1])
    traction = jnp.roll(ordered, me + 1, axis=0)

    newest = jnp.where(me == 0, traction, carried)
    shifted_history = jnp.concatenate([newest[None], history[:-1]], axis=0)
    return (traction, shifted_history)


def solution(mesh):
    in_specs = (
        P("lag", "tile", None, None),
        P("lag", "tile", None, None, None),
        P("tile", None, None),
        P("tile", None, None),
        P("lag", "tile", None),
        P("lag", "tile"),
    )
    out_specs = (P("tile", None, None), P("lag", "tile", None, None))
    return jax.shard_map(shards, mesh=mesh, in_specs=in_specs, out_specs=out_specs, check_vma=False)
```

```python
import jax
import jax.numpy as jnp
from jax import lax
from jax.experimental import pallas as pl
from jax.experimental.pallas import tpu as pltpu
from jax.sharding import PartitionSpec as P

EDGE = 4


def term_kernel(src_ref, cnt_ref, a_ref, *refs):
    *sources, out_ref, acc_ref = refs
    b = pl.program_id(0)
    blocks = pl.num_programs(0)
    lags, slots = a_ref.shape[0], a_ref.shape[1]
    acc_ref[...] = jnp.zeros_like(acc_ref)
    for l in range(lags):
        cnt = cnt_ref[l, b]
        for s in range(slots):
            lf, md, rt = sources[3 * (l * slots + s):3 * (l * slots + s) + 3]
            w = src_ref[l, b, s]
            live = s < cnt
            for ref, cond in ((lf, w < EDGE), (md, (w >= EDGE) & (w < EDGE + blocks)), (rt, w >= EDGE + blocks)):
                @pl.when(live & cond)
                def _():
                    acc_ref[...] += jnp.dot(a_ref[l, s], ref[...], preferred_element_type=jnp.float32)
    out_ref[...] = acc_ref[...].astype(out_ref.dtype)


def lag_partial(history, left, right, lag_blocks, pattern, live_counts):
    lags, blocks, vec, ex = history.shape
    slots = lag_blocks.shape[2]
    window = jnp.arange(blocks, dtype=jnp.int32)[None, :, None] + pattern

    def source_spec(l, s, lo, hi, count):
        def index(b, src, cnt):
            w = src[l, b, s]
            on = (s < cnt[l, b]) & (w >= lo) & (w < hi)
            return (jnp.where(on, l, 0), jnp.where(on, jnp.clip(w - lo, 0, count - 1), 0), 0, 0)
        return pl.BlockSpec((None, None, vec, ex), index)

    in_specs = [pl.BlockSpec((lags, None, slots, vec, vec), lambda b, src, cnt: (0, b, 0, 0, 0))]
    operands = [lag_blocks]
    for l in range(lags):
        for s in range(slots):
            in_specs += [
                source_spec(l, s, 0, EDGE, EDGE),
                source_spec(l, s, EDGE, EDGE + blocks, blocks),
                source_spec(l, s, EDGE + blocks, 2 * EDGE + blocks, EDGE),
            ]
            operands += [left, history, right]
    grid_spec = pltpu.PrefetchScalarGridSpec(
        num_scalar_prefetch=2,
        grid=(blocks,),
        in_specs=in_specs,
        out_specs=pl.BlockSpec((None, vec, ex), lambda b, src, cnt: (b, 0, 0)),
        scratch_shapes=[pltpu.VMEM((vec, ex), jnp.float32)],
    )
    flops = 2 * lags * blocks * slots * vec * vec * ex
    moved = 2 * (lag_blocks.size + slots * history.size + blocks * vec * ex)
    return pl.pallas_call(
        term_kernel,
        grid_spec=grid_spec,
        out_shape=jax.ShapeDtypeStruct((blocks, vec, ex), jnp.bfloat16),
        cost_estimate=pl.CostEstimate(flops=flops, transcendentals=0, bytes_accessed=moved),
    )(window, live_counts, *operands)


def shifted_by(array, axis, by):
    count = lax.axis_size(axis)
    return lax.ppermute(array, axis, [(i, (i + by) % count) for i in range(count)])


def passed_along(array, axis, by):
    length = lax.axis_size(axis)
    pairs = [(i, i + by) for i in range(length) if 0 <= i + by < length]
    return lax.ppermute(array, axis, pairs)


def shards(history, lag_blocks, self_inverse, excitation, pattern, live_counts):
    blocks_here = history.shape[1]
    half = blocks_here // 2
    early = passed_along(history[-1, :half], "lag", 1)
    left = shifted_by(history[:, blocks_here - EDGE:], "tile", 1)
    right = shifted_by(history[:, :EDGE], "tile", -1)
    oldest, left, right, early = lax.optimization_barrier((history[-1, half:], left, right, early))
    late = passed_along(oldest, "lag", 1)
    live = jnp.minimum(live_counts, lag_blocks.shape[2])
    partial = lag_partial(history, left, right, lag_blocks, pattern, live)

    n_lag = lax.axis_size("lag")
    me = lax.axis_index("lag")
    field = lax.dynamic_index_in_dim(partial, me, 0, keepdims=False).astype(jnp.float32)
    for k in range(1, n_lag):
        piece = lax.dynamic_index_in_dim(partial, (me + k) % n_lag, 0, keepdims=False)
        field = field + shifted_by(piece, "lag", k).astype(jnp.float32)
    mine = lax.dynamic_index_in_dim(excitation, me, 0, keepdims=False)
    residual = (mine - field).astype(jnp.bfloat16)
    inverse = lax.dynamic_index_in_dim(self_inverse, me, 0, keepdims=False)
    block = jnp.dot(inverse, residual, preferred_element_type=jnp.float32).astype(jnp.bfloat16)
    block, late = lax.optimization_barrier((block, late))
    carried = jnp.concatenate([early, late], axis=0)
    shifted_history = jnp.concatenate([carried[None], history[:-1]], axis=0)

    gathered = [block] + [shifted_by(block, "lag", k) for k in range(1, n_lag)]
    ordered = jnp.stack(gathered[::-1])
    traction = jnp.roll(ordered, me + 1, axis=0)

    newest = jnp.where(me == 0, traction, carried)
    shifted_history = lax.dynamic_update_slice(shifted_history, newest[None], (0, 0, 0, 0))
    return (traction, shifted_history)


def solution(mesh):
    in_specs = (
        P("lag", "tile", None, None),
        P("lag", "tile", None, None, None),
        P("tile", None, None),
        P("tile", None, None),
        P("lag", "tile", None),
        P("lag", "tile"),
    )
    out_specs = (P("tile", None, None), P("lag", "tile", None, None))
    return jax.shard_map(shards, mesh=mesh, in_specs=in_specs, out_specs=out_specs, check_vma=False)
```

```python
import jax
import jax.numpy as jnp
from jax import lax
from jax.experimental import pallas as pl
from jax.experimental.pallas import tpu as pltpu
from jax.sharding import PartitionSpec as P

EDGE = 4


def term_kernel(src_ref, cnt_ref, a_ref, *refs):
    *sources, out_ref, acc_ref = refs
    b = pl.program_id(0)
    blocks = pl.num_programs(0)
    lags, slots = a_ref.shape[0], a_ref.shape[1]
    acc_ref[...] = jnp.zeros_like(acc_ref)
    for l in range(lags):
        cnt = cnt_ref[l, b]
        for s in range(slots):
            lf, md, rt = sources[3 * (l * slots + s):3 * (l * slots + s) + 3]
            w = src_ref[l, b, s]
            live = s < cnt
            for ref, cond in ((lf, w < EDGE), (md, (w >= EDGE) & (w < EDGE + blocks)), (rt, w >= EDGE + blocks)):
                @pl.when(live & cond)
                def _():
                    acc_ref[...] += jnp.dot(a_ref[l, s], ref[...], preferred_element_type=jnp.float32)
    out_ref[...] = acc_ref[...].astype(out_ref.dtype)


def lag_partial(history, left, right, lag_blocks, pattern, live_counts):
    lags, blocks, vec, ex = history.shape
    slots = lag_blocks.shape[2]
    window = jnp.arange(blocks, dtype=jnp.int32)[None, :, None] + pattern

    def source_spec(l, s, lo, hi, count):
        def index(b, src, cnt):
            w = src[l, b, s]
            on = (s < cnt[l, b]) & (w >= lo) & (w < hi)
            return (jnp.where(on, l, 0), jnp.where(on, jnp.clip(w - lo, 0, count - 1), 0), 0, 0)
        return pl.BlockSpec((None, None, vec, ex), index)

    in_specs = [pl.BlockSpec((lags, None, slots, vec, vec), lambda b, src, cnt: (0, b, 0, 0, 0))]
    operands = [lag_blocks]
    for l in range(lags):
        for s in range(slots):
            in_specs += [
                source_spec(l, s, 0, EDGE, EDGE),
                source_spec(l, s, EDGE, EDGE + blocks, blocks),
                source_spec(l, s, EDGE + blocks, 2 * EDGE + blocks, EDGE),
            ]
            operands += [left, history, right]
    grid_spec = pltpu.PrefetchScalarGridSpec(
        num_scalar_prefetch=2,
        grid=(blocks,),
        in_specs=in_specs,
        out_specs=pl.BlockSpec((None, vec, ex), lambda b, src, cnt: (b, 0, 0)),
        scratch_shapes=[pltpu.VMEM((vec, ex), jnp.float32)],
    )
    flops = 2 * lags * blocks * slots * vec * vec * ex
    moved = 2 * (lag_blocks.size + slots * history.size + blocks * vec * ex)
    return pl.pallas_call(
        term_kernel,
        grid_spec=grid_spec,
        out_shape=jax.ShapeDtypeStruct((blocks, vec, ex), jnp.bfloat16),
        cost_estimate=pl.CostEstimate(flops=flops, transcendentals=0, bytes_accessed=moved),
    )(window, live_counts, *operands)


def shifted_by(array, axis, by):
    count = lax.axis_size(axis)
    return lax.ppermute(array, axis, [(i, (i + by) % count) for i in range(count)])


def passed_along(array, axis, by):
    length = lax.axis_size(axis)
    pairs = [(i, i + by) for i in range(length) if 0 <= i + by < length]
    return lax.ppermute(array, axis, pairs)


def shards(history, lag_blocks, self_inverse, excitation, pattern, live_counts):
    blocks_here = history.shape[1]
    left = shifted_by(history[:, blocks_here - EDGE:], "tile", 1)
    right = shifted_by(history[:, :EDGE], "tile", -1)
    oldest, left, right = lax.optimization_barrier((history[-1], left, right))
    late = passed_along(oldest, "lag", 1)
    live = jnp.minimum(live_counts, lag_blocks.shape[2])
    partial = lag_partial(history, left, right, lag_blocks, pattern, live)

    n_lag = lax.axis_size("lag")
    me = lax.axis_index("lag")
    field = lax.dynamic_index_in_dim(partial, me, 0, keepdims=False).astype(jnp.float32)
    for k in range(1, n_lag):
        piece = lax.dynamic_index_in_dim(partial, (me + k) % n_lag, 0, keepdims=False)
        field = field + shifted_by(piece, "lag", k).astype(jnp.float32)
    mine = lax.dynamic_index_in_dim(excitation, me, 0, keepdims=False)
    residual = (mine - field).astype(jnp.bfloat16)
    inverse = lax.dynamic_index_in_dim(self_inverse, me, 0, keepdims=False)
    block = jnp.dot(inverse, residual, preferred_element_type=jnp.float32).astype(jnp.bfloat16)
    block, late = lax.optimization_barrier((block, late))
    carried = late

    gathered = [block] + [shifted_by(block, "lag", k) for k in range(1, n_lag)]
    ordered = jnp.stack(gathered[::-1])
    traction = jnp.roll(ordered, me + 1, axis=0)

    newest = jnp.where(me == 0, traction, carried)
    shifted_history = jnp.concatenate([newest[None], history[:-1]], axis=0)
    return (traction, shifted_history)


def solution(mesh):
    in_specs = (
        P("lag", "tile", None, None),
        P("lag", "tile", None, None, None),
        P("tile", None, None),
        P("tile", None, None),
        P("lag", "tile", None),
        P("lag", "tile"),
    )
    out_specs = (P("tile", None, None), P("lag", "tile", None, None))
    return jax.shard_map(shards, mesh=mesh, in_specs=in_specs, out_specs=out_specs, check_vma=False)
```
